256 devices in a mesh: blk: 128 (over x, z, y_hi, core), grp: 2 (over y_lo).
Axes of the slice: x: 4, y: 4 (y_hi: 2, y_lo: 2; y = y_hi * 2 + y_lo), z: 8, core: 2. Of those that a mesh axis runs over, the one named last changes fastest.
Arguments:
- raw: bfloat16 [32, 8192, 2400], P(None, ('blk', 'grp')), may hold values from -1200 to 1200
- partner: int32 [3, 128], replicated, may hold values from 0 to 127, as said below
Outputs:
- cross: bfloat16 [3, 256, 8192, 128], P(None, 'grp', 'blk')
The draws below stay inside these ranges and needn't reach their ends.
Inputs may be any that keep to these rules, and one draw needn't show every extreme that they name: Each row pairs off the 128 blocks: no block is its own partner, and the partner of a block's partner is the block itself. No two rows are equal.
All inputs are finite; a program needn't handle non-finite values.
Results may differ from the reference program's by a relative error of at most 0.0065.
Values may be sent and summed in bfloat16 or wider, within the bound.
No kernel may reach another device: no remote copies, remote signals or barrier semaphores. Data moves between devices by JAX's collectives and lax.ppermute only.
A program may use at most 128 MiB of HBM per device.

```python
import math
import jax
import jax.numpy as jnp
from jax import lax

L = 2400
F = 256
SEG = 32
BCH = 64
ROUNDS = 3
CHANNELS = 8192
N_BLK = 128


def draw_raw(key, part):
    key_base = jax.random.fold_in(key, 11)
    key_chan = jax.random.fold_in(key, 12)
    key_seg = jax.random.fold_in(key, 13)
    chan_scale = jnp.exp(jax.random.uniform(key_chan, (1, CHANNELS, 1), jnp.float32) * math.log(10.0))
    seg_scale = jnp.exp(jax.random.uniform(key_seg, (SEG, 1, 1), jnp.float32) * math.log(10.0))
    base_noise = jnp.clip(jax.random.normal(key_base, (SEG, CHANNELS, L), jnp.float32), -6.0, 6.0)
    return (base_noise * chan_scale * seg_scale).astype(jnp.bfloat16)


def draw_partner(key, part):
    relabel = jax.random.permutation(jax.random.fold_in(key, 21), N_BLK).astype(jnp.int32)
    round_pick = jax.random.permutation(jax.random.fold_in(key, 22), N_BLK - 1)[:ROUNDS].astype(jnp.int32)
    modulus = N_BLK - 1
    slot_index = jnp.arange(N_BLK, dtype=jnp.int32)[None, :]
    round_col = round_pick[:, None]
    mirrored = jnp.mod(2 * round_col - slot_index, modulus)
    paired = jnp.where(slot_index == modulus, round_col, jnp.where(mirrored == slot_index, modulus, mirrored))
    return jnp.zeros((ROUNDS, N_BLK), jnp.int32).at[:, relabel].set(relabel[paired])


def setup_inputs(seed: int = 0) -> dict:
    arg_keys = jax.random.split(jax.random.key(seed), 3)
    raw = draw_raw(jax.random.fold_in(arg_keys[2], 71), 0)
    partner = draw_partner(jax.random.fold_in(arg_keys[2], 71), 0)
    return dict(raw=raw, partner=partner)


first_bin = 8
epsilon = 1e-06

def dft_table(length, num_bins):
    sample_idx = lax.broadcasted_iota(jnp.int32, (length, num_bins), 0)
    bin_index = lax.broadcasted_iota(jnp.int32, (length, num_bins), 1) + first_bin
    phase_angle = (sample_idx * bin_index % length).astype(jnp.float32) * (2.0 * math.pi / length)
    return jnp.concatenate([jnp.cos(phase_angle), -jnp.sin(phase_angle)], axis=1).astype(jnp.bfloat16)

def whiten(samples, num_bins):
    seg_count, chan_count, length = samples.shape
    spectrum = jnp.dot(samples.reshape(seg_count * chan_count, length), dft_table(length, num_bins), preferred_element_type=jnp.float32).reshape(seg_count, chan_count, 2 * num_bins)
    real_part = spectrum[:, :, :num_bins]
    imag_part = spectrum[:, :, num_bins:]
    bin_power = lax.optimization_barrier(jnp.mean(real_part * real_part + imag_part * imag_part, axis=0))
    factor = lax.rsqrt(bin_power + epsilon)
    joined = jnp.concatenate([real_part * factor, imag_part * factor], axis=0)
    return jnp.transpose(joined, (2, 1, 0)).astype(jnp.bfloat16)

def reference(raw, partner):

    def block_white(index):
        block = lax.dynamic_slice_in_dim(raw, index * BCH, BCH, 1)
        return whiten(block, F)
    white_all = lax.map(block_white, jnp.arange(N_BLK, dtype=jnp.int32))
    norm_scale = 1.0 / math.sqrt(SEG)

    def round_cross(row):

        def bin_cross(bin_index):
            mine = white_all[:, bin_index].astype(jnp.float32)
            other = mine[row]
            flipped = jnp.concatenate([mine[..., SEG:], -mine[..., :SEG]], axis=-1)
            real_sum = jnp.einsum('bis,bjs->bij', mine, other)
            imag_sum = jnp.einsum('bis,bjs->bij', flipped, other)
            joined = jnp.concatenate([real_sum, imag_sum], axis=-1) * norm_scale
            return joined.reshape(N_BLK * BCH, 2 * BCH).astype(jnp.bfloat16)
        return lax.map(bin_cross, jnp.arange(F, dtype=jnp.int32))
    return lax.map(round_cross, partner)
```

```python
import math

import jax
import jax.numpy as jnp
from jax import lax
from jax.sharding import PartitionSpec as P

F = 256


first_bin = 8
epsilon = 1e-06


def dft_table(length, num_bins):
    sample_idx = lax.broadcasted_iota(jnp.int32, (length, num_bins), 0)
    bin_index = lax.broadcasted_iota(jnp.int32, (length, num_bins), 1) + first_bin
    phase_angle = (sample_idx * bin_index % length).astype(jnp.float32) * (2.0 * math.pi / length)
    return jnp.concatenate([jnp.cos(phase_angle), -jnp.sin(phase_angle)], axis=1).astype(
        jnp.bfloat16
    )


def whiten(samples, num_bins):
    seg_count, chan_count, length = samples.shape
    spectrum = jnp.dot(
        samples.reshape(seg_count * chan_count, length),
        dft_table(length, num_bins),
        preferred_element_type=jnp.float32,
    ).reshape(seg_count, chan_count, 2 * num_bins)
    real_part = spectrum[:, :, :num_bins]
    imag_part = spectrum[:, :, num_bins:]
    bin_power = jnp.mean(real_part * real_part + imag_part * imag_part, axis=0)
    factor = lax.rsqrt(bin_power + epsilon)
    joined = jnp.concatenate([real_part * factor, imag_part * factor], axis=0)
    return jnp.transpose(joined, (2, 1, 0)).astype(jnp.bfloat16)


def per_device(raw, partner):
    spectra = whiten(raw, F)
    halves = lax.all_to_all(spectra, "grp", split_axis=0, concat_axis=1, tiled=True)
    owned = lax.all_to_all(halves[:, None], "blk", split_axis=0, concat_axis=1, tiled=True)
    seg_count = owned.shape[-1] // 2
    norm_scale = 1.0 / math.sqrt(seg_count)
    gathered = jnp.transpose(jnp.take(owned, partner, axis=1), (1, 2, 0, 3, 4))
    other = lax.all_to_all(gathered, "blk", split_axis=1, concat_axis=2, tiled=True)[:, 0]
    turned = jnp.concatenate([-other[..., seg_count:], other[..., :seg_count]], axis=-1)
    both = jnp.concatenate([other, turned], axis=2)
    result = jnp.einsum("fcs,rfjs->rfcj", halves, both, preferred_element_type=jnp.float32)
    return (result * norm_scale).astype(jnp.bfloat16)


def solution(mesh):
    placed = (P(None, ("blk", "grp"), None), P())
    return jax.shard_map(
        per_device,
        mesh=mesh,
        in_specs=placed,
        out_specs=P(None, "grp", "blk", None),
        check_vma=False,
    )
```

```python
import math

import jax
import jax.numpy as jnp
from jax import lax
from jax.sharding import PartitionSpec as P

F = 256


first_bin = 8
epsilon = 1e-06


def dft_table(length, num_bins):
    sample_idx = lax.broadcasted_iota(jnp.int32, (length, num_bins), 0)
    bin_index = lax.broadcasted_iota(jnp.int32, (length, num_bins), 1) + first_bin
    phase_angle = (sample_idx * bin_index % length).astype(jnp.float32) * (2.0 * math.pi / length)
    return jnp.concatenate([jnp.cos(phase_angle), -jnp.sin(phase_angle)], axis=1).astype(
        jnp.bfloat16
    )


def whiten(samples, num_bins):
    seg_count, chan_count, length = samples.shape
    spectrum = jnp.dot(
        samples.reshape(seg_count * chan_count, length),
        dft_table(length, num_bins),
        preferred_element_type=jnp.float32,
    ).reshape(seg_count, chan_count, 2 * num_bins)
    real_part = spectrum[:, :, :num_bins]
    imag_part = spectrum[:, :, num_bins:]
    bin_power = jnp.mean(real_part * real_part + imag_part * imag_part, axis=0)
    factor = lax.rsqrt(bin_power + epsilon)
    joined = jnp.concatenate([real_part * factor, imag_part * factor], axis=0)
    return jnp.transpose(joined, (2, 1, 0)).astype(jnp.bfloat16)


def per_device(raw, partner):
    n_grp = lax.axis_size("grp")
    n_blk = lax.axis_size("blk")
    g = lax.axis_index("grp")
    spectra = whiten(raw, F)
    n_bin, half_ch, two_seg = spectra.shape
    seg_count = two_seg // 2
    own_bins = n_bin // n_grp
    per_owner = own_bins // n_blk
    norm_scale = 1.0 / math.sqrt(seg_count)
    by_grp = spectra.reshape(n_grp, own_bins, half_ch * two_seg)

    mine = lax.dynamic_index_in_dim(by_grp, g, 0, keepdims=False)
    theirs = lax.ppermute(
        lax.dynamic_index_in_dim(by_grp, 1 - g, 0, keepdims=False),
        "grp",
        [(i, (i + 1) % n_grp) for i in range(n_grp)],
    )
    pair = jnp.stack([mine, theirs])
    own = jnp.where(g == 0, pair, pair[::-1])
    own = jnp.transpose(own.reshape(n_grp, own_bins, half_ch, two_seg), (1, 0, 2, 3))
    own = own.reshape(own_bins, n_grp * half_ch, two_seg)

    order = by_grp.reshape(n_grp, n_blk, per_owner, half_ch * two_seg)
    order = jnp.transpose(order, (1, 0, 2, 3)).reshape(n_blk * n_grp * per_owner, half_ch * two_seg)
    owned = lax.all_to_all(order, ("blk", "grp"), split_axis=0, concat_axis=0, tiled=True)
    owned = owned.reshape(n_blk, n_grp, per_owner, half_ch * two_seg)
    owned = jnp.transpose(owned, (0, 2, 1, 3)).reshape(n_blk, per_owner * n_grp * half_ch * two_seg)

    rounds = partner.shape[0]
    gathered = jnp.take(owned, partner.reshape(-1), axis=0)
    gathered = gathered.reshape(rounds, n_blk, per_owner * n_grp * half_ch * two_seg)
    gathered = jnp.transpose(gathered, (1, 0, 2))
    other = lax.all_to_all(gathered, "blk", split_axis=0, concat_axis=0, tiled=True)
    other = other.reshape(n_blk, rounds, per_owner, n_grp * half_ch, two_seg)
    other = jnp.transpose(other, (1, 0, 2, 3, 4)).reshape(rounds, own_bins, n_grp * half_ch, two_seg)

    turned = jnp.concatenate([-other[..., seg_count:], other[..., :seg_count]], axis=-1)
    both = jnp.concatenate([other, turned], axis=2)
    result = jnp.einsum("fcs,rfjs->rfcj", own, both, preferred_element_type=jnp.float32)
    return (result * norm_scale).astype(jnp.bfloat16)


def solution(mesh):
    placed = (P(None, ("blk", "grp"), None), P())
    return jax.shard_map(
        per_device,
        mesh=mesh,
        in_specs=placed,
        out_specs=P(None, "grp", "blk", None),
        check_vma=False,
    )
```

```python
import math

import jax
import jax.numpy as jnp
from jax import lax
from jax.sharding import PartitionSpec as P

F = 256


first_bin = 8
epsilon = 1e-06


def phase_table(step, rows, num_bins, length):
    sample_idx = lax.broadcasted_iota(jnp.int32, (rows, num_bins), 0) * step
    bin_index = lax.broadcasted_iota(jnp.int32, (rows, num_bins), 1) + first_bin
    phase_angle = (sample_idx * bin_index % length).astype(jnp.float32) * (2.0 * math.pi / length)
    return jnp.cos(phase_angle), jnp.sin(phase_angle)


def dft_table(length, num_bins):
    step = 48 if length % 48 == 0 else 1
    cos_c, sin_c = phase_table(step, length // step, num_bins, length)
    cos_f, sin_f = phase_table(1, step, num_bins, length)
    cos_t = cos_c[:, None] * cos_f[None] - sin_c[:, None] * sin_f[None]
    sin_t = sin_c[:, None] * cos_f[None] + cos_c[:, None] * sin_f[None]
    table = jnp.concatenate([cos_t, -sin_t], axis=-1).reshape(length, 2 * num_bins)
    return table.astype(jnp.bfloat16)


def whiten(samples, num_bins):
    seg_count, chan_count, length = samples.shape
    spectrum = jnp.dot(
        samples.reshape(seg_count * chan_count, length),
        dft_table(length, num_bins),
        preferred_element_type=jnp.float32,
    ).reshape(seg_count, chan_count, 2 * num_bins)
    real_part = spectrum[:, :, :num_bins]
    imag_part = spectrum[:, :, num_bins:]
    bin_power = jnp.mean(real_part * real_part + imag_part * imag_part, axis=0)
    factor = lax.rsqrt(bin_power + epsilon)
    joined = jnp.concatenate([real_part * factor, imag_part * factor], axis=0)
    return jnp.transpose(joined, (2, 1, 0)).astype(jnp.bfloat16)


def per_device(raw, partner):
    n_blk = lax.axis_size("blk")
    spectra = whiten(raw, F)
    n_bin, half_ch, two_seg = spectra.shape
    seg_count = two_seg // 2
    norm_scale = 1.0 / math.sqrt(seg_count)
    halves = lax.all_to_all(
        spectra.reshape(n_bin, half_ch * two_seg), "grp", split_axis=0, concat_axis=1, tiled=True
    )
    own_bins, record = halves.shape
    per_owner = own_bins // n_blk
    owned = lax.all_to_all(
        halves.reshape(n_blk, per_owner * record), "blk", split_axis=0, concat_axis=0, tiled=True
    )
    rounds = partner.shape[0]
    gathered = jnp.take(owned, partner.reshape(-1), axis=0, mode="clip")
    gathered = jnp.transpose(gathered.reshape(rounds, n_blk, per_owner * record), (1, 0, 2))
    other = lax.all_to_all(gathered, "blk", split_axis=0, concat_axis=0, tiled=True)
    block_ch = record // two_seg
    other = other.reshape(n_blk, rounds, per_owner, block_ch, two_seg)
    other = jnp.transpose(other, (1, 0, 2, 3, 4)).reshape(rounds, own_bins, block_ch, two_seg)

    own = halves.reshape(own_bins, block_ch, two_seg)
    turned = jnp.concatenate([-other[..., seg_count:], other[..., :seg_count]], axis=-1)
    both = jnp.concatenate([other, turned], axis=2)
    result = jnp.einsum("fcs,rfjs->rfcj", own, both, preferred_element_type=jnp.float32)
    return (result * norm_scale).astype(jnp.bfloat16)


def solution(mesh):
    placed = (P(None, ("blk", "grp"), None), P())
    return jax.shard_map(
        per_device,
        mesh=mesh,
        in_specs=placed,
        out_specs=P(None, "grp", "blk", None),
        check_vma=False,
    )
```

```python
import math

import jax
import jax.numpy as jnp
from jax import lax
from jax.experimental import pallas as pl
from jax.experimental.pallas import tpu as pltpu
from jax.sharding import PartitionSpec as P

F = 256
INTERPRET = False


first_bin = 8
epsilon = 1e-06


def phase_table(step, rows, num_bins, length):
    sample_idx = lax.broadcasted_iota(jnp.int32, (rows, num_bins), 0) * step
    bin_index = lax.broadcasted_iota(jnp.int32, (rows, num_bins), 1) + first_bin
    phase_angle = (sample_idx * bin_index % length).astype(jnp.float32) * (2.0 * math.pi / length)
    return jnp.cos(phase_angle), jnp.sin(phase_angle)


def dft_table(length, num_bins):
    step = 48 if length % 48 == 0 else 1
    cos_c, sin_c = phase_table(step, length // step, num_bins, length)
    cos_f, sin_f = phase_table(1, step, num_bins, length)
    cos_t = cos_c[:, None] * cos_f[None] - sin_c[:, None] * sin_f[None]
    sin_t = sin_c[:, None] * cos_f[None] + cos_c[:, None] * sin_f[None]
    table = jnp.concatenate([cos_t, -sin_t], axis=-1).reshape(length, 2 * num_bins)
    return table.astype(jnp.bfloat16)


def whiten(samples, num_bins):
    seg_count, chan_count, length = samples.shape
    spectrum = jnp.dot(
        samples.reshape(seg_count * chan_count, length),
        dft_table(length, num_bins),
        preferred_element_type=jnp.float32,
    ).reshape(seg_count, chan_count, 2 * num_bins)
    real_part = spectrum[:, :, :num_bins]
    imag_part = spectrum[:, :, num_bins:]
    bin_power = jnp.mean(real_part * real_part + imag_part * imag_part, axis=0)
    factor = lax.rsqrt(bin_power + epsilon)
    joined = jnp.stack([real_part * factor, imag_part * factor], axis=1)
    return jnp.transpose(joined, (3, 0, 1, 2)).astype(jnp.bfloat16)


def cross_kernel(scale, ar_ref, ai_ref, rec_ref, out_ref):
    bins, rounds = rec_ref.shape[0], rec_ref.shape[1]
    width = out_ref.shape[-1]
    lane = lax.broadcasted_iota(jnp.int32, out_ref.shape[2:], 1)
    sign = jnp.where(lane < width // 2, scale, -scale).astype(jnp.float32)
    for f in range(bins):
        ar = ar_ref[f]
        ai = ai_ref[f]
        for r in range(rounds):
            rec = rec_ref[f, r]
            p1 = jnp.dot(ar, rec, preferred_element_type=jnp.float32)
            p2 = jnp.dot(ai, rec, preferred_element_type=jnp.float32)
            out = pltpu.roll(p2, width // 2, 1) * scale + p1 * sign
            out_ref[r, f] = out.astype(out_ref.dtype)


def cross(ar, ai, rec, scale):
    own_bins, block_ch, seg_count = ar.shape
    rounds, width = rec.shape[1], rec.shape[-1]
    fb = 8
    return pl.pallas_call(
        lambda *refs: cross_kernel(scale, *refs),
        grid=(own_bins // fb,),
        in_specs=[
            pl.BlockSpec((fb, block_ch, seg_count), lambda i: (i, 0, 0)),
            pl.BlockSpec((fb, block_ch, seg_count), lambda i: (i, 0, 0)),
            pl.BlockSpec((fb, rounds, seg_count, width), lambda i: (i, 0, 0, 0)),
        ],
        out_specs=pl.BlockSpec((rounds, fb, block_ch, width), lambda i: (0, i, 0, 0)),
        out_shape=jax.ShapeDtypeStruct((rounds, own_bins, block_ch, width), jnp.bfloat16),
        interpret=INTERPRET,
    )(ar, ai, rec)


def per_device(raw, partner):
    n_blk = lax.axis_size("blk")
    n_grp = lax.axis_size("grp")
    spectra = whiten(raw, F)
    n_bin, seg_count, two, half_ch = spectra.shape
    norm_scale = 1.0 / math.sqrt(seg_count)
    halves = lax.all_to_all(
        spectra[:, :, :, None], "grp", split_axis=0, concat_axis=3, tiled=True
    )
    own_bins = halves.shape[0]
    block_ch = n_grp * half_ch
    halves = halves.reshape(own_bins, seg_count, two, block_ch)
    width = two * block_ch
    per_owner = own_bins // n_blk
    owned = lax.all_to_all(
        halves.reshape(n_blk, per_owner * seg_count, width), "blk", split_axis=0, concat_axis=0, tiled=True
    )
    rounds = partner.shape[0]
    gathered = jnp.take(owned, jnp.transpose(partner).reshape(-1), axis=0, mode="clip")
    gathered = gathered.reshape(n_blk, rounds, per_owner, seg_count, width)
    gathered = jnp.transpose(gathered, (0, 2, 1, 3, 4)).reshape(n_blk, per_owner * rounds * seg_count, width)
    other = lax.all_to_all(gathered, "blk", split_axis=0, concat_axis=0, tiled=True)
    other = other.reshape(own_bins, rounds, seg_count, width)

    ar = jnp.transpose(halves[:, :, 0, :], (0, 2, 1))
    ai = jnp.transpose(halves[:, :, 1, :], (0, 2, 1))
    return cross(ar, ai, other, norm_scale)


def solution(mesh):
    placed = (P(None, ("blk", "grp"), None), P())
    return jax.shard_map(
        per_device,
        mesh=mesh,
        in_specs=placed,
        out_specs=P(None, "grp", "blk", None),
        check_vma=False,
    )
```

```python
import math

import jax
import jax.numpy as jnp
from jax import lax
from jax.experimental import pallas as pl
from jax.experimental.pallas import tpu as pltpu
from jax.sharding import PartitionSpec as P

F = 256
INTERPRET = False


first_bin = 8
epsilon = 1e-06


def phase_table(step, rows, num_bins, length):
    sample_idx = lax.broadcasted_iota(jnp.int32, (rows, num_bins), 0) * step
    bin_index = lax.broadcasted_iota(jnp.int32, (rows, num_bins), 1) + first_bin
    phase_angle = (sample_idx * bin_index % length).astype(jnp.float32) * (2.0 * math.pi / length)
    return jnp.cos(phase_angle), jnp.sin(phase_angle)


def dft_table(length, num_bins):
    step = 48 if length % 48 == 0 else 1
    cos_c, sin_c = phase_table(step, length // step, num_bins, length)
    cos_f, sin_f = phase_table(1, step, num_bins, length)
    cos_t = cos_c[:, None] * cos_f[None] - sin_c[:, None] * sin_f[None]
    sin_t = sin_c[:, None] * cos_f[None] + cos_c[:, None] * sin_f[None]
    table = jnp.concatenate([cos_t, -sin_t], axis=-1).reshape(length, 2 * num_bins)
    return table.astype(jnp.bfloat16)


def whiten(samples, num_bins):
    seg_count, chan_count, length = samples.shape
    spectrum = jnp.dot(
        samples.reshape(seg_count * chan_count, length),
        dft_table(length, num_bins),
        preferred_element_type=jnp.float32,
    ).reshape(seg_count, chan_count, 2 * num_bins)
    real_part = spectrum[:, :, :num_bins]
    imag_part = spectrum[:, :, num_bins:]
    bin_power = jnp.mean(real_part * real_part + imag_part * imag_part, axis=0)
    factor = lax.rsqrt(bin_power + epsilon)
    joined = jnp.stack([real_part * factor, imag_part * factor], axis=0)
    return jnp.transpose(joined, (3, 2, 0, 1)).astype(jnp.bfloat16)


def cross_kernel(scale, ar_ref, ai_ref, rec_ref, out_ref):
    bins, rounds = rec_ref.shape[0], rec_ref.shape[1]
    width = out_ref.shape[-1]
    lane = lax.broadcasted_iota(jnp.int32, out_ref.shape[2:], 1)
    sign = jnp.where(lane < width // 2, scale, -scale).astype(jnp.float32)
    for f in range(bins):
        ar = ar_ref[f]
        ai = ai_ref[f]
        for r in range(rounds):
            rec = rec_ref[f, r]
            p1 = jnp.dot(ar, rec, preferred_element_type=jnp.float32)
            p2 = jnp.dot(ai, rec, preferred_element_type=jnp.float32)
            out = pltpu.roll(p2, width // 2, 1) * scale + p1 * sign
            out_ref[r, f] = out.astype(out_ref.dtype)


def cross(ar, ai, rec, scale):
    own_bins, block_ch, seg_count = ar.shape
    rounds, width = rec.shape[1], rec.shape[-1]
    fb = 8
    return pl.pallas_call(
        lambda *refs: cross_kernel(scale, *refs),
        grid=(own_bins // fb,),
        in_specs=[
            pl.BlockSpec((fb, block_ch, seg_count), lambda i: (i, 0, 0)),
            pl.BlockSpec((fb, block_ch, seg_count), lambda i: (i, 0, 0)),
            pl.BlockSpec((fb, rounds, seg_count, width), lambda i: (i, 0, 0, 0)),
        ],
        out_specs=pl.BlockSpec((rounds, fb, block_ch, width), lambda i: (0, i, 0, 0)),
        out_shape=jax.ShapeDtypeStruct((rounds, own_bins, block_ch, width), jnp.bfloat16),
        interpret=INTERPRET,
    )(ar, ai, rec)


def per_device(raw, partner):
    n_blk = lax.axis_size("blk")
    n_grp = lax.axis_size("grp")
    spectra = whiten(raw, F)
    n_bin, half_ch, two, seg_count = spectra.shape
    norm_scale = 1.0 / math.sqrt(seg_count)
    halves = lax.all_to_all(
        spectra.reshape(n_bin, half_ch * two * seg_count), "grp", split_axis=0, concat_axis=1, tiled=True
    )
    own_bins = halves.shape[0]
    block_ch = n_grp * half_ch
    halves = halves.reshape(own_bins, block_ch, two, seg_count)
    ar = halves[:, :, 0, :]
    ai = halves[:, :, 1, :]
    halves = jnp.transpose(halves, (0, 3, 2, 1))
    width = two * block_ch
    per_owner = own_bins // n_blk
    owned = lax.all_to_all(
        halves.reshape(n_blk, per_owner * seg_count, width), "blk", split_axis=0, concat_axis=0, tiled=True
    )
    rounds = partner.shape[0]
    gathered = jnp.take(owned, jnp.transpose(partner).reshape(-1), axis=0, mode="clip")
    gathered = gathered.reshape(n_blk, rounds, per_owner, seg_count, width)
    gathered = jnp.transpose(gathered, (0, 2, 1, 3, 4)).reshape(n_blk, per_owner * rounds * seg_count, width)
    other = lax.all_to_all(gathered, "blk", split_axis=0, concat_axis=0, tiled=True)
    other = other.reshape(own_bins, rounds, seg_count, width)

    return cross(ar, ai, other, norm_scale)


def solution(mesh):
    placed = (P(None, ("blk", "grp"), None), P())
    return jax.shard_map(
        per_device,
        mesh=mesh,
        in_specs=placed,
        out_specs=P(None, "grp", "blk", None),
        check_vma=False,
    )
```

```python
import math

import jax
import jax.numpy as jnp
from jax import lax
from jax.experimental import pallas as pl
from jax.experimental.pallas import tpu as pltpu
from jax.sharding import PartitionSpec as P

F = 256
INTERPRET = False


first_bin = 8
epsilon = 1e-06


def phase_table(step, rows, num_bins, length):
    sample_idx = lax.broadcasted_iota(jnp.int32, (rows, num_bins), 0) * step
    bin_index = lax.broadcasted_iota(jnp.int32, (rows, num_bins), 1) + first_bin
    phase_angle = (sample_idx * bin_index % length).astype(jnp.float32) * (2.0 * math.pi / length)
    return jnp.cos(phase_angle), jnp.sin(phase_angle)


def dft_table(length, num_bins):
    step = 48 if length % 48 == 0 else 1
    cos_c, sin_c = phase_table(step, length // step, num_bins, length)
    cos_f, sin_f = phase_table(1, step, num_bins, length)
    cos_t = cos_c[:, None] * cos_f[None] - sin_c[:, None] * sin_f[None]
    sin_t = sin_c[:, None] * cos_f[None] + cos_c[:, None] * sin_f[None]
    table = jnp.concatenate([cos_t, -sin_t], axis=-1).reshape(length, 2 * num_bins)
    return table.astype(jnp.bfloat16)


def whiten(samples, num_bins):
    seg_count, chan_count, length = samples.shape
    spectrum = jnp.dot(
        samples.reshape(seg_count * chan_count, length),
        dft_table(length, num_bins),
        preferred_element_type=jnp.float32,
    ).reshape(seg_count, chan_count, 2 * num_bins)
    real_part = spectrum[:, :, :num_bins]
    imag_part = spectrum[:, :, num_bins:]
    bin_power = jnp.mean(real_part * real_part + imag_part * imag_part, axis=0)
    factor = lax.rsqrt(bin_power + epsilon)
    joined = jnp.stack([real_part * factor, imag_part * factor], axis=0)
    return jnp.transpose(joined, (3, 2, 0, 1)).astype(jnp.bfloat16)


def cross_kernel(scale, a_ref, rec_ref, out_ref):
    bins, rounds = rec_ref.shape[0], rec_ref.shape[1]
    block_ch, width = out_ref.shape[2], out_ref.shape[3]
    lane = lax.broadcasted_iota(jnp.int32, (block_ch, width), 1)
    sign = jnp.where(lane < width // 2, scale, -scale).astype(jnp.float32)
    for f in range(bins):
        a = a_ref[f]
        for r in range(rounds):
            both = jnp.dot(a, rec_ref[f, r], preferred_element_type=jnp.float32)
            p1 = both[:block_ch]
            p2 = both[block_ch:]
            out = pltpu.roll(p2, width // 2, 1) * scale + p1 * sign
            out_ref[r, f] = out.astype(out_ref.dtype)


def cross(a, rec, scale):
    own_bins, two_ch, seg_count = a.shape
    rounds, width = rec.shape[1], rec.shape[-1]
    block_ch = two_ch // 2
    fb = 16
    return pl.pallas_call(
        lambda *refs: cross_kernel(scale, *refs),
        grid=(own_bins // fb,),
        in_specs=[
            pl.BlockSpec((fb, two_ch, seg_count), lambda i: (i, 0, 0)),
            pl.BlockSpec((fb, rounds, seg_count, width), lambda i: (i, 0, 0, 0)),
        ],
        out_specs=pl.BlockSpec((rounds, fb, block_ch, width), lambda i: (0, i, 0, 0)),
        out_shape=jax.ShapeDtypeStruct((rounds, own_bins, block_ch, width), jnp.bfloat16),
        interpret=INTERPRET,
    )(a, rec)


def per_device(raw, partner):
    n_blk = lax.axis_size("blk")
    n_grp = lax.axis_size("grp")
    spectra = whiten(raw, F)
    n_bin, half_ch, two, seg_count = spectra.shape
    norm_scale = 1.0 / math.sqrt(seg_count)
    halves = lax.all_to_all(
        spectra.reshape(n_bin, half_ch * two * seg_count), "grp", split_axis=0, concat_axis=1, tiled=True
    )
    own_bins = halves.shape[0]
    block_ch = n_grp * half_ch
    halves = halves.reshape(own_bins, block_ch, two, seg_count)
    own = jnp.transpose(halves, (0, 2, 1, 3)).reshape(own_bins, two * block_ch, seg_count)
    halves = jnp.transpose(halves, (0, 3, 2, 1))
    width = two * block_ch
    per_owner = own_bins // n_blk
    owned = lax.all_to_all(
        halves.reshape(n_blk, per_owner * seg_count, width), "blk", split_axis=0, concat_axis=0, tiled=True
    )
    rounds = partner.shape[0]
    gathered = jnp.take(owned, jnp.transpose(partner).reshape(-1), axis=0, mode="clip")
    gathered = gathered.reshape(n_blk, rounds, per_owner, seg_count, width)
    gathered = jnp.transpose(gathered, (0, 2, 1, 3, 4)).reshape(n_blk, per_owner * rounds * seg_count, width)
    other = lax.all_to_all(gathered, "blk", split_axis=0, concat_axis=0, tiled=True)
    other = other.reshape(own_bins, rounds, seg_count, width)

    return cross(own, other, norm_scale)


def solution(mesh):
    placed = (P(None, ("blk", "grp"), None), P())
    return jax.shard_map(
        per_device,
        mesh=mesh,
        in_specs=placed,
        out_specs=P(None, "grp", "blk", None),
        check_vma=False,
    )
```

```python
import math

import jax
import jax.numpy as jnp
from jax import lax
from jax.experimental import pallas as pl
from jax.experimental.pallas import tpu as pltpu
from jax.sharding import PartitionSpec as P

F = 256
INTERPRET = False


first_bin = 8
epsilon = 1e-06


def phase_table(step, rows, num_bins, length):
    sample_idx = lax.broadcasted_iota(jnp.int32, (rows, num_bins), 0) * step
    bin_index = lax.broadcasted_iota(jnp.int32, (rows, num_bins), 1) + first_bin
    phase_angle = (sample_idx * bin_index % length).astype(jnp.float32) * (2.0 * math.pi / length)
    return jnp.cos(phase_angle), jnp.sin(phase_angle)


def dft_table(length, num_bins):
    step = 48 if length % 48 == 0 else 1
    cos_c, sin_c = phase_table(step, length // step, num_bins, length)
    cos_f, sin_f = phase_table(1, step, num_bins, length)
    cos_t = cos_c[:, None] * cos_f[None] - sin_c[:, None] * sin_f[None]
    sin_t = sin_c[:, None] * cos_f[None] + cos_c[:, None] * sin_f[None]
    table = jnp.concatenate([cos_t, -sin_t], axis=-1).reshape(length, 2 * num_bins)
    return table.astype(jnp.bfloat16)


def whiten(samples, num_bins):
    seg_count, chan_count, length = samples.shape
    spectrum = jnp.dot(
        samples.reshape(seg_count * chan_count, length),
        dft_table(length, num_bins),
        preferred_element_type=jnp.float32,
    ).reshape(seg_count, chan_count, 2 * num_bins)
    real_part = spectrum[:, :, :num_bins]
    imag_part = spectrum[:, :, num_bins:]
    bin_power = jnp.mean(real_part * real_part + imag_part * imag_part, axis=0)
    factor = lax.rsqrt(bin_power + epsilon)
    joined = jnp.stack([real_part * factor, imag_part * factor], axis=0)
    return jnp.transpose(joined, (3, 2, 0, 1)).astype(jnp.bfloat16)


def cross_kernel(scale, a_ref, rec_ref, out_ref):
    bins, rounds = rec_ref.shape[0], rec_ref.shape[1]
    block_ch, width = out_ref.shape[2], out_ref.shape[3]
    lane = lax.broadcasted_iota(jnp.int32, (block_ch, width), 1)
    sign = jnp.where(lane < width // 2, scale, -scale).astype(jnp.float32)
    for f in range(bins):
        a = a_ref[f]
        for r in range(rounds):
            both = jnp.dot(a, rec_ref[f, r], preferred_element_type=jnp.float32)
            p1 = both[:block_ch]
            p2 = both[block_ch:]
            out = pltpu.roll(p2, width // 2, 1) * scale + p1 * sign
            out_ref[r, f] = out.astype(out_ref.dtype)


def cross(a, rec, scale):
    own_bins, two_ch, seg_count = a.shape
    rounds, width = rec.shape[1], rec.shape[-1]
    block_ch = two_ch // 2
    fb = 16
    return pl.pallas_call(
        lambda *refs: cross_kernel(scale, *refs),
        grid=(own_bins // fb,),
        in_specs=[
            pl.BlockSpec((fb, two_ch, seg_count), lambda i: (i, 0, 0)),
            pl.BlockSpec((fb, rounds, seg_count, width), lambda i: (i, 0, 0, 0)),
        ],
        out_specs=pl.BlockSpec((rounds, fb, block_ch, width), lambda i: (0, i, 0, 0)),
        out_shape=jax.ShapeDtypeStruct((rounds, own_bins, block_ch, width), jnp.bfloat16),
        interpret=INTERPRET,
    )(a, rec)


def per_device(raw, partner):
    n_blk = lax.axis_size("blk")
    n_grp = lax.axis_size("grp")
    spectra = whiten(raw, F)
    n_bin, half_ch, two, seg_count = spectra.shape
    norm_scale = 1.0 / math.sqrt(seg_count)
    halves = lax.all_to_all(
        spectra.reshape(n_bin, half_ch * two * seg_count), "grp", split_axis=0, concat_axis=1, tiled=True
    )
    own_bins = halves.shape[0]
    block_ch = n_grp * half_ch
    halves = halves.reshape(own_bins, block_ch, two, seg_count)
    own = jnp.transpose(halves, (0, 2, 1, 3)).reshape(own_bins, two * block_ch, seg_count)
    width = two * block_ch
    per_owner = own_bins // n_blk
    order = spectra.reshape(n_grp, n_blk, per_owner, half_ch * two * seg_count)
    order = jnp.transpose(order, (1, 0, 2, 3)).reshape(n_bin, half_ch * two * seg_count)
    owned = lax.all_to_all(order, ("blk", "grp"), split_axis=0, concat_axis=0, tiled=True)
    owned = owned.reshape(n_blk, n_grp, per_owner, half_ch, two, seg_count)
    owned = jnp.transpose(owned, (0, 2, 5, 4, 1, 3)).reshape(n_blk, per_owner * seg_count, width)
    rounds = partner.shape[0]
    gathered = jnp.take(owned, jnp.transpose(partner).reshape(-1), axis=0, mode="clip")
    gathered = gathered.reshape(n_blk, rounds, per_owner, seg_count, width)
    gathered = jnp.transpose(gathered, (0, 2, 1, 3, 4)).reshape(n_blk, per_owner * rounds * seg_count, width)
    other = lax.all_to_all(gathered, "blk", split_axis=0, concat_axis=0, tiled=True)
    other = other.reshape(own_bins, rounds, seg_count, width)

    return cross(own, other, norm_scale)


def solution(mesh):
    placed = (P(None, ("blk", "grp"), None), P())
    return jax.shard_map(
        per_device,
        mesh=mesh,
        in_specs=placed,
        out_specs=P(None, "grp", "blk", None),
        check_vma=False,
    )
```

```python
import math

import jax
import jax.numpy as jnp
from jax import lax
from jax.experimental import pallas as pl
from jax.experimental.pallas import tpu as pltpu
from jax.sharding import PartitionSpec as P

F = 256
INTERPRET = False


first_bin = 8
epsilon = 1e-06


def phase_table(step, rows, num_bins, length):
    sample_idx = lax.broadcasted_iota(jnp.int32, (rows, num_bins), 0) * step
    bin_index = lax.broadcasted_iota(jnp.int32, (rows, num_bins), 1) + first_bin
    phase_angle = (sample_idx * bin_index % length).astype(jnp.float32) * (2.0 * math.pi / length)
    return jnp.cos(phase_angle), jnp.sin(phase_angle)


def dft_table(length, num_bins):
    step = 48 if length % 48 == 0 else 1
    cos_c, sin_c = phase_table(step, length // step, num_bins, length)
    cos_f, sin_f = phase_table(1, step, num_bins, length)
    cos_t = cos_c[:, None] * cos_f[None] - sin_c[:, None] * sin_f[None]
    sin_t = sin_c[:, None] * cos_f[None] + cos_c[:, None] * sin_f[None]
    table = jnp.concatenate([cos_t, -sin_t], axis=-1).reshape(length, 2 * num_bins)
    return table.astype(jnp.bfloat16)


def whiten(samples, num_bins):
    seg_count, chan_count, length = samples.shape
    spectrum = jnp.dot(
        samples.reshape(seg_count * chan_count, length),
        dft_table(length, num_bins),
        preferred_element_type=jnp.float32,
    ).reshape(seg_count, chan_count, 2 * num_bins)
    real_part = spectrum[:, :, :num_bins]
    imag_part = spectrum[:, :, num_bins:]
    bin_power = jnp.mean(real_part * real_part + imag_part * imag_part, axis=0)
    factor = lax.rsqrt(bin_power + epsilon)
    joined = jnp.stack([real_part * factor, imag_part * factor], axis=0)
    return jnp.transpose(joined, (3, 2, 0, 1)).astype(jnp.bfloat16)


def cross_kernel(scale, a_ref, rec_ref, out_ref):
    bins, rounds = rec_ref.shape[0], rec_ref.shape[1]
    block_ch, width = out_ref.shape[2], out_ref.shape[3]
    lane = lax.broadcasted_iota(jnp.int32, (block_ch, width), 1)
    sign = jnp.where(lane < width // 2, scale, -scale).astype(jnp.float32)
    for f in range(bins):
        a = a_ref[f]
        for r in range(rounds):
            both = jnp.dot(a, rec_ref[f, r], preferred_element_type=jnp.float32)
            p1 = both[:block_ch]
            p2 = both[block_ch:]
            out = pltpu.roll(p2, width // 2, 1) * scale + p1 * sign
            out_ref[r, f] = out.astype(out_ref.dtype)


def cross(a, rec, scale):
    own_bins, two_ch, seg_count = a.shape
    rounds, width = rec.shape[1], rec.shape[-1]
    block_ch = two_ch // 2
    fb = 16
    return pl.pallas_call(
        lambda *refs: cross_kernel(scale, *refs),
        grid=(own_bins // fb,),
        in_specs=[
            pl.BlockSpec((fb, two_ch, seg_count), lambda i: (i, 0, 0)),
            pl.BlockSpec((fb, rounds, seg_count, width), lambda i: (i, 0, 0, 0)),
        ],
        out_specs=pl.BlockSpec((rounds, fb, block_ch, width), lambda i: (0, i, 0, 0)),
        out_shape=jax.ShapeDtypeStruct((rounds, own_bins, block_ch, width), jnp.bfloat16),
        interpret=INTERPRET,
    )(a, rec)


def per_device(raw, partner):
    n_blk = lax.axis_size("blk")
    n_grp = lax.axis_size("grp")
    spectra = whiten(raw, F)
    n_bin, half_ch, two, seg_count = spectra.shape
    norm_scale = 1.0 / math.sqrt(seg_count)
    g = lax.axis_index("grp")
    own_bins = n_bin // n_grp
    by_grp = spectra.reshape(n_grp, own_bins, half_ch * two * seg_count)
    mine = lax.dynamic_index_in_dim(by_grp, g, 0, keepdims=False)
    theirs = lax.ppermute(
        lax.dynamic_index_in_dim(by_grp, 1 - g, 0, keepdims=False),
        "grp",
        [(i, (i + 1) % n_grp) for i in range(n_grp)],
    )
    first = jnp.where(g == 0, mine, theirs)
    second = jnp.where(g == 0, theirs, mine)
    halves = jnp.stack([first, second], axis=1)
    block_ch = n_grp * half_ch
    halves = halves.reshape(own_bins, block_ch, two, seg_count)
    own = jnp.transpose(halves, (0, 2, 1, 3)).reshape(own_bins, two * block_ch, seg_count)
    halves = jnp.transpose(halves, (0, 3, 2, 1))
    width = two * block_ch
    per_owner = own_bins // n_blk
    owned = lax.all_to_all(
        halves.reshape(n_blk, per_owner * seg_count, width), "blk", split_axis=0, concat_axis=0, tiled=True
    )
    rounds = partner.shape[0]
    gathered = jnp.take(owned, jnp.transpose(partner).reshape(-1), axis=0, mode="clip")
    gathered = gathered.reshape(n_blk, rounds, per_owner, seg_count, width)
    gathered = jnp.transpose(gathered, (0, 2, 1, 3, 4)).reshape(n_blk, per_owner * rounds * seg_count, width)
    other = lax.all_to_all(gathered, "blk", split_axis=0, concat_axis=0, tiled=True)
    other = other.reshape(own_bins, rounds, seg_count, width)

    return cross(own, other, norm_scale)


def solution(mesh):
    placed = (P(None, ("blk", "grp"), None), P())
    return jax.shard_map(
        per_device,
        mesh=mesh,
        in_specs=placed,
        out_specs=P(None, "grp", "blk", None),
        check_vma=False,
    )
```

```python
import math

import jax
import jax.numpy as jnp
from jax import lax
from jax.experimental import pallas as pl
from jax.experimental.pallas import tpu as pltpu
from jax.sharding import PartitionSpec as P

F = 256
INTERPRET = False


first_bin = 8
epsilon = 1e-06


def phase_table(step, rows, num_bins, length):
    sample_idx = lax.broadcasted_iota(jnp.int32, (rows, num_bins), 0) * step
    bin_index = lax.broadcasted_iota(jnp.int32, (rows, num_bins), 1) + first_bin
    phase_angle = (sample_idx * bin_index % length).astype(jnp.float32) * (2.0 * math.pi / length)
    return jnp.cos(phase_angle), jnp.sin(phase_angle)


def dft_table(length, num_bins):
    step = 48 if length % 48 == 0 else 1
    cos_c, sin_c = phase_table(step, length // step, num_bins, length)
    cos_f, sin_f = phase_table(1, step, num_bins, length)
    cos_t = cos_c[:, None] * cos_f[None] - sin_c[:, None] * sin_f[None]
    sin_t = sin_c[:, None] * cos_f[None] + cos_c[:, None] * sin_f[None]
    table = jnp.concatenate([cos_t, -sin_t], axis=-1).reshape(length, 2 * num_bins)
    return table.astype(jnp.bfloat16)


def whiten(samples, num_bins):
    seg_count, chan_count, length = samples.shape
    spectrum = jnp.dot(
        samples.reshape(seg_count * chan_count, length),
        dft_table(length, num_bins),
        preferred_element_type=jnp.float32,
    ).reshape(seg_count, chan_count, 2 * num_bins)
    real_part = spectrum[:, :, :num_bins]
    imag_part = spectrum[:, :, num_bins:]
    bin_power = jnp.mean(real_part * real_part + imag_part * imag_part, axis=0)
    factor = lax.rsqrt(bin_power + epsilon)
    joined = jnp.stack([real_part * factor, imag_part * factor], axis=0)
    return jnp.transpose(joined, (3, 2, 0, 1)).astype(jnp.bfloat16)


def cross_kernel(scale, a_ref, rec_ref, out_ref):
    bins, rounds = rec_ref.shape[0], rec_ref.shape[1]
    block_ch, width = out_ref.shape[2], out_ref.shape[3]
    lane = lax.broadcasted_iota(jnp.int32, (block_ch, width), 1)
    sign = jnp.where(lane < width // 2, scale, -scale).astype(jnp.float32)
    for f in range(bins):
        rhs = jnp.concatenate([rec_ref[f, r] for r in range(rounds)], axis=1)
        both = jnp.dot(a_ref[f], rhs, preferred_element_type=jnp.float32)
        for r in range(rounds):
            p1 = both[:block_ch, r * width:(r + 1) * width]
            p2 = both[block_ch:, r * width:(r + 1) * width]
            out = pltpu.roll(p2, width // 2, 1) * scale + p1 * sign
            out_ref[r, f] = out.astype(out_ref.dtype)


def cross(a, rec, scale):
    own_bins, two_ch, seg_count = a.shape
    rounds, width = rec.shape[1], rec.shape[-1]
    block_ch = two_ch // 2
    fb = 32
    return pl.pallas_call(
        lambda *refs: cross_kernel(scale, *refs),
        grid=(own_bins // fb,),
        in_specs=[
            pl.BlockSpec((fb, two_ch, seg_count), lambda i: (i, 0, 0)),
            pl.BlockSpec((fb, rounds, seg_count, width), lambda i: (i, 0, 0, 0)),
        ],
        out_specs=pl.BlockSpec((rounds, fb, block_ch, width), lambda i: (0, i, 0, 0)),
        out_shape=jax.ShapeDtypeStruct((rounds, own_bins, block_ch, width), jnp.bfloat16),
        interpret=INTERPRET,
    )(a, rec)


def per_device(raw, partner):
    n_blk = lax.axis_size("blk")
    n_grp = lax.axis_size("grp")
    spectra = whiten(raw, F)
    n_bin, half_ch, two, seg_count = spectra.shape
    norm_scale = 1.0 / math.sqrt(seg_count)
    halves = lax.all_to_all(
        spectra.reshape(n_bin, half_ch * two * seg_count), "grp", split_axis=0, concat_axis=1, tiled=True
    )
    own_bins = halves.shape[0]
    block_ch = n_grp * half_ch
    halves = halves.reshape(own_bins, block_ch, two, seg_count)
    own = jnp.transpose(halves, (0, 2, 1, 3)).reshape(own_bins, two * block_ch, seg_count)
    halves = jnp.transpose(halves, (0, 3, 2, 1))
    width = two * block_ch
    per_owner = own_bins // n_blk
    owned = lax.all_to_all(
        halves.reshape(n_blk, per_owner * seg_count, width), "blk", split_axis=0, concat_axis=0, tiled=True
    )
    rounds = partner.shape[0]
    gathered = jnp.take(owned, jnp.transpose(partner).reshape(-1), axis=0, mode="clip")
    gathered = gathered.reshape(n_blk, rounds, per_owner, seg_count, width)
    gathered = jnp.transpose(gathered, (0, 2, 1, 3, 4)).reshape(n_blk, per_owner * rounds * seg_count, width)
    other = lax.all_to_all(gathered, "blk", split_axis=0, concat_axis=0, tiled=True)
    other = other.reshape(own_bins, rounds, seg_count, width)

    return cross(own, other, norm_scale)


def solution(mesh):
    placed = (P(None, ("blk", "grp"), None), P())
    return jax.shard_map(
        per_device,
        mesh=mesh,
        in_specs=placed,
        out_specs=P(None, "grp", "blk", None),
        check_vma=False,
    )
```

```python
import math

import jax
import jax.numpy as jnp
from jax import lax
from jax.experimental import pallas as pl
from jax.experimental.pallas import tpu as pltpu
from jax.sharding import PartitionSpec as P

F = 256
INTERPRET = False


first_bin = 8
epsilon = 1e-06


def phase_table(step, rows, num_bins, length, base):
    sample_idx = lax.broadcasted_iota(jnp.int32, (rows, num_bins), 0) * step
    bin_index = lax.broadcasted_iota(jnp.int32, (rows, num_bins), 1) + (first_bin + base)
    phase_angle = (sample_idx * bin_index % length).astype(jnp.float32) * (2.0 * math.pi / length)
    return jnp.cos(phase_angle), jnp.sin(phase_angle)


def dft_table(length, num_bins, base):
    step = 48 if length % 48 == 0 else 1
    cos_c, sin_c = phase_table(step, length // step, num_bins, length, base)
    cos_f, sin_f = phase_table(1, step, num_bins, length, base)
    cos_t = cos_c[:, None] * cos_f[None] - sin_c[:, None] * sin_f[None]
    sin_t = sin_c[:, None] * cos_f[None] + cos_c[:, None] * sin_f[None]
    table = jnp.concatenate([cos_t, -sin_t], axis=-1).reshape(length, 2 * num_bins)
    return table.astype(jnp.bfloat16)


def whiten(samples, num_bins, base):
    seg_count, chan_count, length = samples.shape
    spectrum = jnp.dot(
        samples.reshape(seg_count * chan_count, length),
        dft_table(length, num_bins, base),
        preferred_element_type=jnp.float32,
    ).reshape(seg_count, chan_count, 2 * num_bins)
    real_part = spectrum[:, :, :num_bins]
    imag_part = spectrum[:, :, num_bins:]
    bin_power = jnp.mean(real_part * real_part + imag_part * imag_part, axis=0)
    factor = lax.rsqrt(bin_power + epsilon)
    joined = jnp.stack([real_part * factor, imag_part * factor], axis=0)
    return jnp.transpose(joined, (3, 2, 0, 1)).astype(jnp.bfloat16)


def cross_kernel(scale, a_ref, rec_ref, out_ref):
    bins, rounds = rec_ref.shape[0], rec_ref.shape[1]
    block_ch, width = out_ref.shape[2], out_ref.shape[3]
    lane = lax.broadcasted_iota(jnp.int32, (block_ch, width), 1)
    sign = jnp.where(lane < width // 2, scale, -scale).astype(jnp.float32)
    for f in range(bins):
        rhs = jnp.concatenate([rec_ref[f, r] for r in range(rounds)], axis=1)
        both = jnp.dot(a_ref[f], rhs, preferred_element_type=jnp.float32)
        for r in range(rounds):
            p1 = both[:block_ch, r * width:(r + 1) * width]
            p2 = both[block_ch:, r * width:(r + 1) * width]
            out = pltpu.roll(p2, width // 2, 1) * scale + p1 * sign
            out_ref[r, f] = out.astype(out_ref.dtype)


def cross(a, rec, scale):
    own_bins, two_ch, seg_count = a.shape
    rounds, width = rec.shape[1], rec.shape[-1]
    block_ch = two_ch // 2
    fb = 32
    return pl.pallas_call(
        lambda *refs: cross_kernel(scale, *refs),
        grid=(own_bins // fb,),
        in_specs=[
            pl.BlockSpec((fb, two_ch, seg_count), lambda i: (i, 0, 0)),
            pl.BlockSpec((fb, rounds, seg_count, width), lambda i: (i, 0, 0, 0)),
        ],
        out_specs=pl.BlockSpec((rounds, fb, block_ch, width), lambda i: (0, i, 0, 0)),
        out_shape=jax.ShapeDtypeStruct((rounds, own_bins, block_ch, width), jnp.bfloat16),
        interpret=INTERPRET,
    )(a, rec)


def per_device(raw, partner):
    n_blk = lax.axis_size("blk")
    n_grp = lax.axis_size("grp")
    g = lax.axis_index("grp")
    own_bins = F // n_grp
    sent = whiten(raw, own_bins, (1 - g) * own_bins)
    half_ch, two, seg_count = sent.shape[1:]
    norm_scale = 1.0 / math.sqrt(seg_count)
    theirs = lax.ppermute(
        sent.reshape(own_bins, half_ch * two * seg_count),
        "grp",
        [(i, (i + 1) % n_grp) for i in range(n_grp)],
    )
    mine = whiten(raw, own_bins, g * own_bins).reshape(own_bins, half_ch * two * seg_count)
    first = jnp.where(g == 0, mine, theirs)
    second = jnp.where(g == 0, theirs, mine)
    halves = jnp.stack([first, second], axis=1)
    own_bins = halves.shape[0]
    block_ch = n_grp * half_ch
    halves = halves.reshape(own_bins, block_ch, two, seg_count)
    own = jnp.transpose(halves, (0, 2, 1, 3)).reshape(own_bins, two * block_ch, seg_count)
    halves = jnp.transpose(halves, (0, 3, 2, 1))
    width = two * block_ch
    per_owner = own_bins // n_blk
    owned = lax.all_to_all(
        halves.reshape(n_blk, per_owner * seg_count, width), "blk", split_axis=0, concat_axis=0, tiled=True
    )
    rounds = partner.shape[0]
    gathered = jnp.take(owned, jnp.transpose(partner).reshape(-1), axis=0, mode="clip")
    gathered = gathered.reshape(n_blk, rounds, per_owner, seg_count, width)
    gathered = jnp.transpose(gathered, (0, 2, 1, 3, 4)).reshape(n_blk, per_owner * rounds * seg_count, width)
    other = lax.all_to_all(gathered, "blk", split_axis=0, concat_axis=0, tiled=True)
    other = other.reshape(own_bins, rounds, seg_count, width)

    return cross(own, other, norm_scale)


def solution(mesh):
    placed = (P(None, ("blk", "grp"), None), P())
    return jax.shard_map(
        per_device,
        mesh=mesh,
        in_specs=placed,
        out_specs=P(None, "grp", "blk", None),
        check_vma=False,
    )
```

```python
import math

import jax
import jax.numpy as jnp
from jax import lax
from jax.experimental import pallas as pl
from jax.experimental.pallas import tpu as pltpu
from jax.sharding import PartitionSpec as P

F = 256
INTERPRET = False


first_bin = 8
epsilon = 1e-06


def phase_table(step, rows, num_bins, length, base):
    sample_idx = lax.broadcasted_iota(jnp.int32, (rows, num_bins), 0) * step
    bin_index = lax.broadcasted_iota(jnp.int32, (rows, num_bins), 1) + (first_bin + base)
    phase_angle = (sample_idx * bin_index % length).astype(jnp.float32) * (2.0 * math.pi / length)
    return jnp.cos(phase_angle), jnp.sin(phase_angle)


def dft_table(length, num_bins, base):
    step = 48 if length % 48 == 0 else 1
    cos_c, sin_c = phase_table(step, length // step, num_bins, length, base)
    cos_f, sin_f = phase_table(1, step, num_bins, length, base)
    cos_t = cos_c[:, None] * cos_f[None] - sin_c[:, None] * sin_f[None]
    sin_t = sin_c[:, None] * cos_f[None] + cos_c[:, None] * sin_f[None]
    table = jnp.concatenate([cos_t, -sin_t], axis=-1).reshape(length, 2 * num_bins)
    return table.astype(jnp.bfloat16)


def whiten(samples, num_bins, base):
    seg_count, chan_count, length = samples.shape
    spectrum = jnp.dot(
        samples.reshape(seg_count * chan_count, length),
        dft_table(length, num_bins, base),
        preferred_element_type=jnp.float32,
    ).reshape(seg_count, chan_count, 2 * num_bins)
    real_part = spectrum[:, :, :num_bins]
    imag_part = spectrum[:, :, num_bins:]
    bin_power = jnp.mean(real_part * real_part + imag_part * imag_part, axis=0)
    factor = lax.rsqrt(bin_power + epsilon)
    joined = jnp.stack([real_part * factor, imag_part * factor], axis=0)
    return jnp.transpose(joined, (3, 2, 0, 1)).astype(jnp.bfloat16)


def cross_kernel(scale, a_ref, rec_ref, out_ref):
    bins, rounds = rec_ref.shape[0], rec_ref.shape[1]
    block_ch, width = out_ref.shape[2], out_ref.shape[3]
    lane = lax.broadcasted_iota(jnp.int32, (block_ch, width), 1)
    sign = jnp.where(lane < width // 2, scale, -scale).astype(jnp.float32)
    for f in range(bins):
        rhs = jnp.concatenate([rec_ref[f, r] for r in range(rounds)], axis=1)
        both = jnp.dot(a_ref[f], rhs, preferred_element_type=jnp.float32)
        for r in range(rounds):
            p1 = both[:block_ch, r * width:(r + 1) * width]
            p2 = both[block_ch:, r * width:(r + 1) * width]
            out = pltpu.roll(p2, width // 2, 1) * scale + p1 * sign
            out_ref[r, f] = out.astype(out_ref.dtype)


def cross(a, rec, scale):
    own_bins, two_ch, seg_count = a.shape
    rounds, width = rec.shape[1], rec.shape[-1]
    block_ch = two_ch // 2
    fb = 32
    return pl.pallas_call(
        lambda *refs: cross_kernel(scale, *refs),
        grid=(own_bins // fb,),
        in_specs=[
            pl.BlockSpec((fb, two_ch, seg_count), lambda i: (i, 0, 0)),
            pl.BlockSpec((fb, rounds, seg_count, width), lambda i: (i, 0, 0, 0)),
        ],
        out_specs=pl.BlockSpec((rounds, fb, block_ch, width), lambda i: (0, i, 0, 0)),
        out_shape=jax.ShapeDtypeStruct((rounds, own_bins, block_ch, width), jnp.bfloat16),
        interpret=INTERPRET,
    )(a, rec)


def per_device(raw, partner):
    n_blk = lax.axis_size("blk")
    n_grp = lax.axis_size("grp")
    g = lax.axis_index("grp")
    own_bins = F // n_grp
    pieces = 2 if own_bins % 2 == 0 else 1
    piece = own_bins // pieces
    received = []
    for i in range(pieces):
        sent = whiten(raw, piece, (1 - g) * own_bins + i * piece)
        half_ch, two, seg_count = sent.shape[1:]
        received.append(
            lax.ppermute(
                sent.reshape(piece, half_ch * two * seg_count),
                "grp",
                [(j, (j + 1) % n_grp) for j in range(n_grp)],
            )
        )
    norm_scale = 1.0 / math.sqrt(seg_count)
    theirs = jnp.concatenate(received, axis=0)
    mine = whiten(raw, own_bins, g * own_bins).reshape(own_bins, half_ch * two * seg_count)
    first = jnp.where(g == 0, mine, theirs)
    second = jnp.where(g == 0, theirs, mine)
    halves = jnp.stack([first, second], axis=1)
    own_bins = halves.shape[0]
    block_ch = n_grp * half_ch
    halves = halves.reshape(own_bins, block_ch, two, seg_count)
    own = jnp.transpose(halves, (0, 2, 1, 3)).reshape(own_bins, two * block_ch, seg_count)
    halves = jnp.transpose(halves, (0, 3, 2, 1))
    width = two * block_ch
    per_owner = own_bins // n_blk
    owned = lax.all_to_all(
        halves.reshape(n_blk, per_owner * seg_count, width), "blk", split_axis=0, concat_axis=0, tiled=True
    )
    rounds = partner.shape[0]
    gathered = jnp.take(owned, jnp.transpose(partner).reshape(-1), axis=0, mode="clip")
    gathered = gathered.reshape(n_blk, rounds, per_owner, seg_count, width)
    gathered = jnp.transpose(gathered, (0, 2, 1, 3, 4)).reshape(n_blk, per_owner * rounds * seg_count, width)
    other = lax.all_to_all(gathered, "blk", split_axis=0, concat_axis=0, tiled=True)
    other = other.reshape(own_bins, rounds, seg_count, width)

    return cross(own, other, norm_scale)


def solution(mesh):
    placed = (P(None, ("blk", "grp"), None), P())
    return jax.shard_map(
        per_device,
        mesh=mesh,
        in_specs=placed,
        out_specs=P(None, "grp", "blk", None),
        check_vma=False,
    )
```

```python
import math

import jax
import jax.numpy as jnp
from jax import lax
from jax.experimental import pallas as pl
from jax.experimental.pallas import tpu as pltpu
from jax.sharding import PartitionSpec as P

F = 256
INTERPRET = False


first_bin = 8
epsilon = 1e-06


def phase_table(step, rows, num_bins, length, base):
    sample_idx = lax.broadcasted_iota(jnp.int32, (rows, num_bins), 0) * step
    bin_index = lax.broadcasted_iota(jnp.int32, (rows, num_bins), 1) + (first_bin + base)
    phase_angle = (sample_idx * bin_index % length).astype(jnp.float32) * (2.0 * math.pi / length)
    return jnp.cos(phase_angle), jnp.sin(phase_angle)


def dft_table(length, num_bins, base):
    step = 48 if length % 48 == 0 else 1
    cos_c, sin_c = phase_table(step, length // step, num_bins, length, base)
    cos_f, sin_f = phase_table(1, step, num_bins, length, base)
    cos_t = cos_c[:, None] * cos_f[None] - sin_c[:, None] * sin_f[None]
    sin_t = sin_c[:, None] * cos_f[None] + cos_c[:, None] * sin_f[None]
    table = jnp.concatenate([cos_t, -sin_t], axis=-1).reshape(length, 2 * num_bins)
    return table.astype(jnp.bfloat16)


def whiten(samples, num_bins, base):
    seg_count, chan_count, length = samples.shape
    spectrum = jnp.dot(
        samples.reshape(seg_count * chan_count, length),
        dft_table(length, num_bins, base),
        preferred_element_type=jnp.float32,
    ).reshape(seg_count, chan_count, 2 * num_bins)
    real_part = spectrum[:, :, :num_bins]
    imag_part = spectrum[:, :, num_bins:]
    bin_power = jnp.mean(real_part * real_part + imag_part * imag_part, axis=0)
    factor = lax.rsqrt(bin_power + epsilon)
    joined = jnp.stack([real_part * factor, imag_part * factor], axis=0)
    return jnp.transpose(joined, (3, 2, 0, 1)).astype(jnp.bfloat16)


def cross_kernel(scale, a_ref, rec_ref, out_ref):
    bins, rounds = rec_ref.shape[0], rec_ref.shape[1]
    block_ch, width = out_ref.shape[2], out_ref.shape[3]
    lane = lax.broadcasted_iota(jnp.int32, (block_ch, width), 1)
    sign = jnp.where(lane < width // 2, scale, -scale).astype(jnp.float32)
    for f in range(bins):
        rhs = jnp.concatenate([rec_ref[f, r] for r in range(rounds)], axis=1)
        both = jnp.dot(a_ref[f], rhs, preferred_element_type=jnp.float32)
        for r in range(rounds):
            p1 = both[:block_ch, r * width:(r + 1) * width]
            p2 = both[block_ch:, r * width:(r + 1) * width]
            out = pltpu.roll(p2, width // 2, 1) * scale + p1 * sign
            out_ref[r, f] = out.astype(out_ref.dtype)


def cross(a, rec, scale):
    own_bins, two_ch, seg_count = a.shape
    rounds, width = rec.shape[1], rec.shape[-1]
    block_ch = two_ch // 2
    fb = 32
    return pl.pallas_call(
        lambda *refs: cross_kernel(scale, *refs),
        grid=(own_bins // fb,),
        in_specs=[
            pl.BlockSpec((fb, two_ch, seg_count), lambda i: (i, 0, 0)),
            pl.BlockSpec((fb, rounds, seg_count, width), lambda i: (i, 0, 0, 0)),
        ],
        out_specs=pl.BlockSpec((rounds, fb, block_ch, width), lambda i: (0, i, 0, 0)),
        out_shape=jax.ShapeDtypeStruct((rounds, own_bins, block_ch, width), jnp.bfloat16),
        interpret=INTERPRET,
    )(a, rec)


def per_device(raw, partner):
    n_blk = lax.axis_size("blk")
    n_grp = lax.axis_size("grp")
    g = lax.axis_index("grp")
    own_bins = F // n_grp
    seg_total, chan_total = raw.shape[0], raw.shape[1]
    pieces = 2 if chan_total % 2 == 0 else 1
    piece = chan_total // pieces
    kept = []
    received = []
    for i in range(pieces):
        spec = whiten(raw[:, i * piece:(i + 1) * piece], F, 0)
        half_ch, two, seg_count = spec.shape[1:]
        by_grp = spec.reshape(n_grp, own_bins, piece * two * seg_count)
        kept.append(lax.dynamic_index_in_dim(by_grp, g, 0, keepdims=False))
        received.append(
            lax.ppermute(
                lax.dynamic_index_in_dim(by_grp, 1 - g, 0, keepdims=False),
                "grp",
                [(j, (j + 1) % n_grp) for j in range(n_grp)],
            )
        )
    half_ch = chan_total
    norm_scale = 1.0 / math.sqrt(seg_count)
    mine = jnp.concatenate(kept, axis=1)
    theirs = jnp.concatenate(received, axis=1)
    first = jnp.where(g == 0, mine, theirs)
    second = jnp.where(g == 0, theirs, mine)
    halves = jnp.stack([first, second], axis=1)
    own_bins = halves.shape[0]
    block_ch = n_grp * half_ch
    halves = halves.reshape(own_bins, block_ch, two, seg_count)
    own = jnp.transpose(halves, (0, 2, 1, 3)).reshape(own_bins, two * block_ch, seg_count)
    halves = jnp.transpose(halves, (0, 3, 2, 1))
    width = two * block_ch
    per_owner = own_bins // n_blk
    owned = lax.all_to_all(
        halves.reshape(n_blk, per_owner * seg_count, width), "blk", split_axis=0, concat_axis=0, tiled=True
    )
    rounds = partner.shape[0]
    gathered = jnp.take(owned, jnp.transpose(partner).reshape(-1), axis=0, mode="clip")
    gathered = gathered.reshape(n_blk, rounds, per_owner, seg_count, width)
    gathered = jnp.transpose(gathered, (0, 2, 1, 3, 4)).reshape(n_blk, per_owner * rounds * seg_count, width)
    other = lax.all_to_all(gathered, "blk", split_axis=0, concat_axis=0, tiled=True)
    other = other.reshape(own_bins, rounds, seg_count, width)

    return cross(own, other, norm_scale)


def solution(mesh):
    placed = (P(None, ("blk", "grp"), None), P())
    return jax.shard_map(
        per_device,
        mesh=mesh,
        in_specs=placed,
        out_specs=P(None, "grp", "blk", None),
        check_vma=False,
    )
```

```python
import math

import jax
import jax.numpy as jnp
from jax import lax
from jax.experimental import pallas as pl
from jax.experimental.pallas import tpu as pltpu
from jax.sharding import PartitionSpec as P

F = 256
INTERPRET = False


first_bin = 8
epsilon = 1e-06


def phase_table(step, rows, num_bins, length, base):
    sample_idx = lax.broadcasted_iota(jnp.int32, (rows, num_bins), 0) * step
    bin_index = lax.broadcasted_iota(jnp.int32, (rows, num_bins), 1) + (first_bin + base)
    phase_angle = (sample_idx * bin_index % length).astype(jnp.float32) * (2.0 * math.pi / length)
    return jnp.cos(phase_angle), jnp.sin(phase_angle)


def dft_table(length, num_bins, base):
    step = 48 if length % 48 == 0 else 1
    cos_c, sin_c = phase_table(step, length // step, num_bins, length, base)
    cos_f, sin_f = phase_table(1, step, num_bins, length, base)
    cos_t = cos_c[:, None] * cos_f[None] - sin_c[:, None] * sin_f[None]
    sin_t = sin_c[:, None] * cos_f[None] + cos_c[:, None] * sin_f[None]
    table = jnp.concatenate([cos_t, -sin_t], axis=-1).reshape(length, 2 * num_bins)
    return table.astype(jnp.bfloat16)


def whiten(samples, num_bins, base):
    seg_count, chan_count, length = samples.shape
    spectrum = jnp.dot(
        samples.reshape(seg_count * chan_count, length),
        dft_table(length, num_bins, base),
        preferred_element_type=jnp.float32,
    ).reshape(seg_count, chan_count, 2 * num_bins)
    real_part = spectrum[:, :, :num_bins]
    imag_part = spectrum[:, :, num_bins:]
    bin_power = jnp.mean(real_part * real_part + imag_part * imag_part, axis=0)
    factor = lax.rsqrt(bin_power + epsilon)
    joined = jnp.stack([real_part * factor, imag_part * factor], axis=0)
    return jnp.transpose(joined, (3, 2, 0, 1)).astype(jnp.bfloat16)


def cross_kernel(scale, a_ref, rec_ref, out_ref):
    bins, rounds = rec_ref.shape[0], rec_ref.shape[1]
    block_ch, width = out_ref.shape[2], out_ref.shape[3]
    lane = lax.broadcasted_iota(jnp.int32, (block_ch, width), 1)
    sign = jnp.where(lane < width // 2, scale, -scale).astype(jnp.float32)
    for f in range(bins):
        rhs = jnp.concatenate([rec_ref[f, r] for r in range(rounds)], axis=1)
        both = jnp.dot(a_ref[f], rhs, preferred_element_type=jnp.float32)
        for r in range(rounds):
            p1 = both[:block_ch, r * width:(r + 1) * width]
            p2 = both[block_ch:, r * width:(r + 1) * width]
            out = pltpu.roll(p2, width // 2, 1) * scale + p1 * sign
            out_ref[r, f] = out.astype(out_ref.dtype)


def cross(a, rec, scale):
    own_bins, two_ch, seg_count = a.shape
    rounds, width = rec.shape[1], rec.shape[-1]
    block_ch = two_ch // 2
    fb = 32
    return pl.pallas_call(
        lambda *refs: cross_kernel(scale, *refs),
        grid=(own_bins // fb,),
        in_specs=[
            pl.BlockSpec((fb, two_ch, seg_count), lambda i: (i, 0, 0)),
            pl.BlockSpec((fb, rounds, seg_count, width), lambda i: (i, 0, 0, 0)),
        ],
        out_specs=pl.BlockSpec((rounds, fb, block_ch, width), lambda i: (0, i, 0, 0)),
        out_shape=jax.ShapeDtypeStruct((rounds, own_bins, block_ch, width), jnp.bfloat16),
        interpret=INTERPRET,
    )(a, rec)


def per_device(raw, partner):
    n_blk = lax.axis_size("blk")
    n_grp = lax.axis_size("grp")
    g = lax.axis_index("grp")
    own_bins = F // n_grp
    sent = whiten(raw, own_bins, (1 - g) * own_bins)
    half_ch, two, seg_count = sent.shape[1:]
    norm_scale = 1.0 / math.sqrt(seg_count)
    theirs = lax.ppermute(
        sent.reshape(own_bins, half_ch * two * seg_count),
        "grp",
        [(i, (i + 1) % n_grp) for i in range(n_grp)],
    )
    mine = whiten(raw, own_bins, g * own_bins).reshape(own_bins, half_ch * two * seg_count)
    first = jnp.where(g == 0, mine, theirs)
    second = jnp.where(g == 0, theirs, mine)
    halves = jnp.stack([first, second], axis=1)
    block_ch = n_grp * half_ch
    halves = halves.reshape(own_bins, block_ch, two, seg_count)
    own = jnp.transpose(halves, (0, 2, 1, 3)).reshape(own_bins, two * block_ch, seg_count)
    width = two * block_ch
    per_owner = own_bins // n_blk

    def seg_major(x):
        return jnp.transpose(x.reshape(own_bins, half_ch, two, seg_count), (0, 3, 2, 1))

    rec_mine = seg_major(mine)
    rec_theirs = seg_major(theirs)
    rec = jnp.where(
        g == 0, jnp.stack([rec_mine, rec_theirs], axis=3), jnp.stack([rec_theirs, rec_mine], axis=3)
    )
    owned = lax.all_to_all(
        rec.reshape(n_blk, per_owner * seg_count, width), "blk", split_axis=0, concat_axis=0, tiled=True
    )
    rounds = partner.shape[0]
    gathered = jnp.take(owned, jnp.transpose(partner).reshape(-1), axis=0, mode="clip")
    gathered = gathered.reshape(n_blk, rounds, per_owner, seg_count, width)
    gathered = jnp.transpose(gathered, (0, 2, 1, 3, 4)).reshape(n_blk, per_owner * rounds * seg_count, width)
    other = lax.all_to_all(gathered, "blk", split_axis=0, concat_axis=0, tiled=True)
    other = other.reshape(own_bins, rounds, seg_count, width)

    return cross(own, other, norm_scale)


def solution(mesh):
    placed = (P(None, ("blk", "grp"), None), P())
    return jax.shard_map(
        per_device,
        mesh=mesh,
        in_specs=placed,
        out_specs=P(None, "grp", "blk", None),
        check_vma=False,
    )
```

```python
import math

import jax
import jax.numpy as jnp
from jax import lax
from jax.experimental import pallas as pl
from jax.experimental.pallas import tpu as pltpu
from jax.sharding import PartitionSpec as P

F = 256
INTERPRET = False


first_bin = 8
epsilon = 1e-06


def phase_table(step, rows, num_bins, length, base):
    sample_idx = lax.broadcasted_iota(jnp.int32, (rows, num_bins), 0) * step
    bin_index = lax.broadcasted_iota(jnp.int32, (rows, num_bins), 1) + (first_bin + base)
    phase_angle = (sample_idx * bin_index % length).astype(jnp.float32) * (2.0 * math.pi / length)
    return jnp.cos(phase_angle), jnp.sin(phase_angle)


def dft_table(length, num_bins, base):
    step = 48 if length % 48 == 0 else 1
    cos_c, sin_c = phase_table(step, length // step, num_bins, length, base)
    cos_f, sin_f = phase_table(1, step, num_bins, length, base)
    cos_t = cos_c[:, None] * cos_f[None] - sin_c[:, None] * sin_f[None]
    sin_t = sin_c[:, None] * cos_f[None] + cos_c[:, None] * sin_f[None]
    table = jnp.concatenate([cos_t, -sin_t], axis=-1).reshape(length, 2 * num_bins)
    return table.astype(jnp.bfloat16)


def whiten(samples, num_bins, base):
    seg_count, chan_count, length = samples.shape
    spectrum = jnp.dot(
        samples.reshape(seg_count * chan_count, length),
        dft_table(length, num_bins, base),
        preferred_element_type=jnp.float32,
    ).reshape(seg_count, chan_count, 2 * num_bins)
    real_part = spectrum[:, :, :num_bins]
    imag_part = spectrum[:, :, num_bins:]
    bin_power = jnp.mean(real_part * real_part + imag_part * imag_part, axis=0)
    factor = lax.rsqrt(bin_power + epsilon)
    joined = jnp.stack([real_part * factor, imag_part * factor], axis=0)
    return jnp.transpose(joined, (3, 2, 0, 1)).astype(jnp.bfloat16)


def cross_kernel(scale, a_ref, rec_ref, out_ref):
    bins, rounds = rec_ref.shape[0], rec_ref.shape[1]
    block_ch, width = out_ref.shape[2], out_ref.shape[3]
    lane = lax.broadcasted_iota(jnp.int32, (block_ch, width), 1)
    sign = jnp.where(lane < width // 2, scale, -scale).astype(jnp.float32)
    for f in range(bins):
        rhs = jnp.concatenate([rec_ref[f, r] for r in range(rounds)], axis=1)
        both = jnp.dot(a_ref[f], rhs, preferred_element_type=jnp.float32)
        for r in range(rounds):
            p1 = both[:block_ch, r * width:(r + 1) * width]
            p2 = both[block_ch:, r * width:(r + 1) * width]
            out = pltpu.roll(p2, width // 2, 1) * scale + p1 * sign
            out_ref[r, f] = out.astype(out_ref.dtype)


def cross(a, rec, scale):
    own_bins, two_ch, seg_count = a.shape
    rounds, width = rec.shape[1], rec.shape[-1]
    block_ch = two_ch // 2
    fb = 16
    return pl.pallas_call(
        lambda *refs: cross_kernel(scale, *refs),
        grid=(own_bins // fb,),
        in_specs=[
            pl.BlockSpec((fb, two_ch, seg_count), lambda i: (i, 0, 0)),
            pl.BlockSpec((fb, rounds, seg_count, width), lambda i: (i, 0, 0, 0)),
        ],
        out_specs=pl.BlockSpec((rounds, fb, block_ch, width), lambda i: (0, i, 0, 0)),
        out_shape=jax.ShapeDtypeStruct((rounds, own_bins, block_ch, width), jnp.bfloat16),
        interpret=INTERPRET,
    )(a, rec)


def per_device(raw, partner):
    n_blk = lax.axis_size("blk")
    n_grp = lax.axis_size("grp")
    g = lax.axis_index("grp")
    own_bins = F // n_grp
    sent = whiten(raw, own_bins, (1 - g) * own_bins)
    half_ch, two, seg_count = sent.shape[1:]
    norm_scale = 1.0 / math.sqrt(seg_count)
    theirs = lax.ppermute(
        sent.reshape(own_bins, half_ch * two * seg_count),
        "grp",
        [(i, (i + 1) % n_grp) for i in range(n_grp)],
    )
    mine = whiten(raw, own_bins, g * own_bins).reshape(own_bins, half_ch * two * seg_count)
    first = jnp.where(g == 0, mine, theirs)
    second = jnp.where(g == 0, theirs, mine)
    halves = jnp.stack([first, second], axis=1)
    block_ch = n_grp * half_ch
    halves = halves.reshape(own_bins, block_ch, two, seg_count)
    own = jnp.transpose(halves, (0, 2, 1, 3)).reshape(own_bins, two * block_ch, seg_count)
    width = two * block_ch
    per_owner = own_bins // n_blk

    def seg_major(x):
        return jnp.transpose(x.reshape(own_bins, half_ch, two, seg_count), (0, 3, 2, 1))

    rec_mine = seg_major(mine)
    rec_theirs = seg_major(theirs)
    rec = jnp.where(
        g == 0, jnp.stack([rec_mine, rec_theirs], axis=3), jnp.stack([rec_theirs, rec_mine], axis=3)
    )
    owned = lax.all_to_all(
        rec.reshape(n_blk, per_owner * seg_count, width), "blk", split_axis=0, concat_axis=0, tiled=True
    )
    rounds = partner.shape[0]
    gathered = jnp.take(owned, jnp.transpose(partner).reshape(-1), axis=0, mode="clip")
    gathered = gathered.reshape(n_blk, rounds, per_owner, seg_count, width)
    gathered = jnp.transpose(gathered, (0, 2, 1, 3, 4)).reshape(n_blk, per_owner * rounds * seg_count, width)
    other = lax.all_to_all(gathered, "blk", split_axis=0, concat_axis=0, tiled=True)
    other = other.reshape(own_bins, rounds, seg_count, width)

    return cross(own, other, norm_scale)


def solution(mesh):
    placed = (P(None, ("blk", "grp"), None), P())
    return jax.shard_map(
        per_device,
        mesh=mesh,
        in_specs=placed,
        out_specs=P(None, "grp", "blk", None),
        check_vma=False,
    )
```
